256 devices in a mesh: ctx: 16 (over x, y), tp: 8 (over z), dp: 2 (over core).
Axes of the slice: x: 4, y: 4, z: 8, core: 2. Of those that a mesh axis runs over, the one named last changes fastest.
Arguments:
- attn_out: bfloat16 [32768, 2048], P(('dp', 'ctx'), 'tp'), parts along dimension 0, may hold values from -6 to 6
- routing: int32 [32768, 8], P(('dp', 'ctx', 'tp')), parts along dimension 0, may hold values from 0 to 127, all different within a row; in each aligned block of 128 rows (0 to 127, 128 to 255, ...) at most 12 rows name the same one
- gates: float32 [32768, 8], P(('dp', 'ctx', 'tp')), parts along dimension 0, may hold values from 0.1 to 1
- w_gate: bfloat16 [256, 2048, 768], P(('dp', 'ctx', 'tp')), parts along dimension 0, may hold values from -0.125 to 0.125
- w_up: bfloat16 [256, 2048, 768], P(('dp', 'ctx', 'tp')), parts along dimension 0, may hold values from -0.125 to 0.125
- w_down: bfloat16 [256, 768, 2048], P(('dp', 'ctx', 'tp')), parts along dimension 0, may hold values from -0.21875 to 0.21875
Outputs:
- moe_out: bfloat16 [32768, 2048], P(('dp', 'ctx'), 'tp'), parts along dimension 0
The draws below stay inside these ranges and needn't reach their ends.
There are 2 independent parts, one for each index of `dp`. The reference program is written for one: setup_inputs(seed, part) draws one part's arguments, and reference() takes and returns one part's arrays. A program takes and returns all parts, laid end to end along the dimension named above; each array names one. Nothing has to cross between parts.
Inputs may be any that keep to these rules, and one draw needn't show every extreme that they name: `routing`: each row names 8 different experts. In each aligned block of 128 rows (the rows of one device of ctx and tp), no expert is named by more than 12 rows, a bound that some block reaches.
All inputs are finite; a program needn't handle non-finite values.
Results may differ from the reference program's by a relative error of at most 0.0057.
Values may be sent and summed in bfloat16 or wider, within the bound.
No kernel may reach another device: no remote copies, remote signals or barrier semaphores. Data moves between devices by JAX's collectives and lax.ppermute only.
A program may use at most 192 MiB of HBM per device.

```python
import math
import jax
import jax.numpy as jnp
import numpy as np
from jax import lax

D = 2048
FF = 768
TOP = 8
TOK_DEV = 128
EXPERTS = 128
CAP = 12
TOKENS = 16384
N_CTX = 16
N_TP = 8


def block_levels(key, dims, split, smallest, high):
    level, own = 1.0, jax.random.fold_in(key, 6)
    for axis_at, parts in split:
        steps = jnp.exp(jax.random.uniform(jax.random.fold_in(own, axis_at), (parts,), jnp.float32, smallest / len(split), high / len(split)))
        level = level * jnp.repeat(steps, dims[axis_at] // parts).reshape([-1 if axis == axis_at else 1 for axis in range(len(dims))])
    return level


def assign_block(stream_key, own, number, rows, number_of, top, most, lean):
    sequence = jax.random.permutation(stream_key, number_of)
    packed, usual = shares(number_of, rows * top, most, lean, True), shares(number_of, rows * top, most, lean, False)
    places = jnp.arange(number_of)

    def named(lengths, turn):
        used = int((lengths > 0).sum())
        fixed = max(1, used // 4)
        passed = fixed + (places - fixed + turn * (used - fixed)) % max(1, number_of - fixed)
        return jnp.zeros((number_of,), jnp.int32).at[sequence[jnp.where(places < fixed, places, passed)]].set(jnp.asarray(lengths, jnp.int32))

    lengths = jnp.where(number % 4 == 0, named(packed, number // 4), named(usual, number - number // 4 - 1))
    mixed = jax.random.permutation(jax.random.fold_in(own, 3), number_of)
    source_of, taker = mixed[0:number_of // 2 * 2:2], mixed[1:number_of // 2 * 2:2]
    margin = jnp.minimum(lengths[source_of] - 1, most - lengths[taker]) // 2
    margin = jnp.where((source_of == sequence[0]) | (taker == sequence[0]) | (lengths[taker] == 0), 0, jnp.maximum(margin, 0))
    passed = jax.random.randint(jax.random.fold_in(own, 4), (number_of // 2,), 0, 1 << 20) % (margin + 1)
    lengths = lengths.at[source_of].add(-passed).at[taker].add(passed)
    members = jnp.searchsorted(jnp.cumsum(lengths), jnp.arange(rows * top), side="right").astype(jnp.int32)
    grid = members.reshape(top, rows).T
    grid = grid[jax.random.permutation(jax.random.fold_in(own, 1), rows)]
    turn = jax.random.randint(jax.random.fold_in(own, 2), (rows, 1), 0, top)
    return jnp.take_along_axis(grid, (jnp.arange(top)[None, :] + turn) % top, axis=1)


def shares(amount, total, reach, lean, full):
    portions = [(1 << 20) // math.isqrt(rank ** lean) + 1 for rank in range(1, amount + 1)]
    largest = reach if full else min(reach, max(-(-total // amount), total * portions[0] // sum(portions)))
    least = 1 if total - largest >= amount - 1 else 0
    given, surplus = [largest] + [least] * (amount - 1), total - largest - least * (amount - 1)
    while surplus > 0:
        movable = [i for i in range(1, amount) if given[i] < largest] or [i for i in range(1, amount) if given[i] < reach]
        pool, budget = sum([portions[i] for i in movable]), surplus
        for i in movable:
            addition = min(reach - given[i], max(1, budget * portions[i] // pool), surplus)
            given[i] = given[i] + addition
            surplus = surplus - addition
    return np.array(given)


def noise(rng, shape, scale, bound, shards=(), kind=jnp.bfloat16):
    level = block_levels(rng, shape, shards, -0.22, 0.18) if shards else 1.0
    result = jax.random.normal(rng, shape, jnp.float32) * scale * level
    return jnp.minimum(jnp.maximum(result, -bound), bound).astype(kind)


def setup_inputs(seed: int = 0, part: int = 0) -> dict:
    seeds = jax.random.split(jax.random.key(seed), 7)
    part_splits = jax.random.split(jax.random.fold_in(seeds[6], part), 7)
    attn_out = noise(part_splits[0], (TOKENS, D), 1.0, 6.0, ((0, 16), (1, 8)))
    routing_keys = jax.random.split(jax.random.fold_in(part_splits[1], 1), TOKENS // TOK_DEV)
    routing_turns = jax.random.permutation(jax.random.fold_in(part_splits[1], 3), TOKENS // TOK_DEV)
    routing = jax.vmap(lambda own, number: assign_block(jax.random.fold_in(part_splits[1], 2), own, number, TOK_DEV, EXPERTS, TOP, CAP, 2))(routing_keys, routing_turns).reshape((TOKENS, TOP))
    gates = jnp.clip(0.1 + 0.9 * jax.random.uniform(part_splits[2], (TOKENS, TOP), jnp.float32) ** block_levels(part_splits[2], (TOKENS, TOP), ((0, 128),), -0.2, 0.2), 0.1, 1.0)
    w_gate = noise(part_splits[3], (EXPERTS, D, FF), D ** -0.5, 0.125, ((0, 128),))
    w_up = noise(part_splits[4], (EXPERTS, D, FF), D ** -0.5, 0.125, ((0, 128),))
    w_down = noise(part_splits[5], (EXPERTS, FF, D), FF ** -0.5, 0.21875, ((0, 128),))
    return dict(attn_out=attn_out, routing=routing, gates=gates, w_gate=w_gate, w_up=w_up, w_down=w_down)


def expert_block(features, gate_mat, up_mat, down_mat):
    gate_proj = jnp.dot(features, gate_mat, preferred_element_type=jnp.float32)
    up_proj = jnp.dot(features, up_mat, preferred_element_type=jnp.float32)
    hidden = (jax.nn.silu(gate_proj) * up_proj).astype(jnp.bfloat16)
    return jnp.dot(hidden, down_mat, preferred_element_type=jnp.float32).astype(jnp.bfloat16)


def reference(attn_out, routing, gates, w_gate, w_up, w_down):
    blocks = N_CTX * N_TP
    expert_ids = routing.reshape(blocks, TOK_DEV * TOP).astype(jnp.int32)
    one_hot = (expert_ids[:, :, None] == jnp.arange(EXPERTS, dtype=jnp.int32)[None, None, :]).astype(jnp.int32)
    slot_of = jnp.sum(jnp.cumsum(one_hot, axis=1) * one_hot, axis=2) - 1
    block_index = jnp.arange(blocks, dtype=jnp.int32)[:, None]
    target = (expert_ids * blocks + block_index) * CAP + slot_of
    source_row = block_index * TOK_DEV + jnp.arange(TOK_DEV * TOP, dtype=jnp.int32)[None, :] // TOP
    slot_table = jnp.full((EXPERTS * blocks * CAP,), -1, jnp.int32)
    slot_table = slot_table.at[target.reshape(-1)].set(source_row.reshape(-1).astype(jnp.int32))
    slot_table = slot_table.reshape(EXPERTS, blocks * CAP)

    def serve(operands):
        indices, gate_mat, up_mat, down_mat = operands
        picked = attn_out[jnp.maximum(indices, 0)]
        features = jnp.where((indices >= 0)[:, None], picked, jnp.zeros((), attn_out.dtype))
        return expert_block(features, gate_mat, up_mat, down_mat)

    outputs = lax.map(serve, (slot_table, w_gate, w_up, w_down))
    flat_out = outputs.reshape(EXPERTS * blocks * CAP, D)
    token_target = target.reshape(TOKENS, TOP)
    total = jnp.zeros((TOKENS, D), jnp.float32)
    for which in range(TOP):
        total = total + gates[:, which:which + 1] * flat_out[token_target[:, which]].astype(jnp.float32)
    return total.astype(jnp.bfloat16)
```

```python
import jax
import jax.numpy as jnp
from jax import lax
from jax.sharding import PartitionSpec as P


def slot_numbers(expert_ids, experts):
    one_hot = (
        expert_ids[:, :, None] == jnp.arange(experts, dtype=jnp.int32)[None, None, :]
    ).astype(jnp.int32)
    return jnp.sum(jnp.cumsum(one_hot, axis=1) * one_hot, axis=2) - 1


def expert_rows(features, w_gate, w_up, w_down, form):
    hidden_form = form[:-1] + "f"
    gate_proj = jnp.einsum(
        form + ",ldf->" + hidden_form, features, w_gate, preferred_element_type=jnp.float32
    )
    up_proj = jnp.einsum(
        form + ",ldf->" + hidden_form, features, w_up, preferred_element_type=jnp.float32
    )
    hidden = (jax.nn.silu(gate_proj) * up_proj).astype(jnp.bfloat16)
    result = jnp.einsum(
        hidden_form + ",lfd->" + form, hidden, w_down, preferred_element_type=jnp.float32
    )
    return result.astype(jnp.bfloat16)


def on_device(attn_out, routing, gates, w_gate, w_up, w_down):
    n_ctx = lax.axis_size("ctx")
    n_tp = lax.axis_size("tp")
    me_tp = lax.axis_index("tp")
    exp_dev = w_gate.shape[0]
    experts = exp_dev * n_ctx * n_tp
    tok_blk, top_count = routing.shape
    width = attn_out.shape[1] * n_tp
    capacity = 3 * tok_blk * top_count // (2 * experts)

    slot_of = slot_numbers(routing.reshape(1, tok_blk * top_count), experts)
    code = routing * capacity + slot_of.reshape(tok_blk, top_count)
    info = jnp.concatenate([code.astype(jnp.float32), gates], axis=1)
    info_all = lax.all_gather(info, "tp", axis=0)
    code_all = info_all[:, :, :top_count].astype(jnp.int32)
    gates_all = info_all[:, :, top_count:]
    expert_all = code_all // capacity
    slot_all = code_all - expert_all * capacity
    dest_ctx = expert_all // (n_tp * exp_dev)
    dest_tp = (expert_all // exp_dev) % n_tp
    dest_loc = expert_all % exp_dev
    mine = dest_tp == me_tp
    per_dest = exp_dev * capacity
    position = jnp.where(mine, (dest_ctx * exp_dev + dest_loc) * capacity + slot_all, -1)
    slots_all = n_ctx * per_dest
    hits = position[..., None] == jnp.arange(slots_all, dtype=jnp.int32)
    select = jnp.sum(hits.astype(jnp.int32), axis=2).astype(jnp.bfloat16)
    weight = jnp.sum(jnp.where(hits, gates_all[..., None], 0.0), axis=2)

    feats = lax.all_gather(attn_out, "tp", axis=0)
    feats = feats.reshape(n_tp, n_tp, tok_blk, width // n_tp)
    select = select.reshape(n_tp, tok_blk, n_ctx, per_dest)
    outgoing = jnp.einsum(
        "bjcq,sbjf->cbqsf", select, feats, preferred_element_type=jnp.bfloat16
    ).reshape(n_ctx, n_tp * per_dest, width)

    received = lax.all_to_all(outgoing, "ctx", split_axis=0, concat_axis=0, tiled=True)
    rows = received.reshape(n_ctx, n_tp, exp_dev, capacity, width)
    rows = jnp.transpose(rows, (2, 0, 1, 3, 4)).reshape(exp_dev, n_ctx * n_tp * capacity, width)
    result = expert_rows(rows, w_gate, w_up, w_down, "lsd")
    result = jnp.transpose(
        result.reshape(exp_dev, n_ctx, n_tp, capacity, width), (1, 2, 0, 3, 4)
    ).reshape(n_ctx, n_tp * per_dest, width)
    returned = lax.all_to_all(result, "ctx", split_axis=0, concat_axis=0, tiled=True)
    returned = returned.reshape(n_ctx, n_tp, per_dest, width)

    weight = weight.reshape(n_tp, tok_blk, n_ctx, per_dest)
    w_hi = weight.astype(jnp.bfloat16)
    w_lo = (weight - w_hi.astype(jnp.float32)).astype(jnp.bfloat16)
    partial = jnp.einsum(
        "bjcq,cbqd->bjd", w_hi, returned, preferred_element_type=jnp.float32
    ) + jnp.einsum("bjcq,cbqd->bjd", w_lo, returned, preferred_element_type=jnp.float32)
    partial = partial.reshape(n_tp * tok_blk, width)
    total = lax.psum_scatter(partial, "tp", scatter_dimension=1, tiled=True)
    return total.astype(jnp.bfloat16)


def solution(mesh):
    in_specs = (
        P(("dp", "ctx"), "tp"),
        P(("dp", "ctx", "tp"), None),
        P(("dp", "ctx", "tp"), None),
        P(("dp", "ctx", "tp"), None, None),
        P(("dp", "ctx", "tp"), None, None),
        P(("dp", "ctx", "tp"), None, None),
    )
    out_specs = P(("dp", "ctx"), "tp")
    return jax.shard_map(
        on_device, mesh=mesh, in_specs=in_specs, out_specs=out_specs, check_vma=False
    )
```

```python
import jax
import jax.numpy as jnp
from jax import lax
from jax.sharding import PartitionSpec as P

CHUNKS = 2


def slot_numbers(expert_ids, experts):
    one_hot = (
        expert_ids[:, :, None] == jnp.arange(experts, dtype=jnp.int32)[None, None, :]
    ).astype(jnp.int32)
    return jnp.sum(jnp.cumsum(one_hot, axis=1) * one_hot, axis=2) - 1


def expert_rows(features, w_gate, w_up, w_down, form):
    hidden_form = form[:-1] + "f"
    gate_proj = jnp.einsum(
        form + ",ldf->" + hidden_form, features, w_gate, preferred_element_type=jnp.float32
    )
    up_proj = jnp.einsum(
        form + ",ldf->" + hidden_form, features, w_up, preferred_element_type=jnp.float32
    )
    hidden = (jax.nn.silu(gate_proj) * up_proj).astype(jnp.bfloat16)
    result = jnp.einsum(
        hidden_form + ",lfd->" + form, hidden, w_down, preferred_element_type=jnp.float32
    )
    return result.astype(jnp.bfloat16)


def bf16_part(x):
    return lax.reduce_precision(x, exponent_bits=8, mantissa_bits=7)


def on_device(attn_out, routing, gates, w_gate, w_up, w_down):
    n_ctx = lax.axis_size("ctx")
    n_tp = lax.axis_size("tp")
    me_tp = lax.axis_index("tp")
    exp_dev = w_gate.shape[0]
    experts = exp_dev * n_ctx * n_tp
    tok_blk, top = routing.shape
    cols = attn_out.shape[1]
    width = cols * n_tp
    capacity = 3 * tok_blk * top // (2 * experts)
    per_dest = exp_dev * capacity

    slot_of = slot_numbers(routing.reshape(1, tok_blk * top), experts).reshape(tok_blk, top)
    g1 = bf16_part(gates)
    rest = gates - g1
    g2 = bf16_part(rest)
    g3 = rest - g2
    info = jnp.concatenate(
        [routing.astype(jnp.float32), slot_of.astype(jnp.float32), g1, g2, g3], axis=1
    ).astype(jnp.bfloat16)
    info_cols = 64
    info = jnp.pad(info, ((0, 0), (0, info_cols - info.shape[1])))
    info_rows = tok_blk * info_cols // cols
    info = info.reshape(info_rows, cols)

    blk_chunk = n_tp // CHUNKS
    rows_chunk = blk_chunk * tok_blk
    outs = []
    for h in range(CHUNKS):
        piece = attn_out[h * rows_chunk:(h + 1) * rows_chunk]
        if h == 0:
            piece = jnp.concatenate([piece, info], axis=0)
        gathered = lax.all_gather(piece, "tp", axis=1, tiled=True)
        feats = gathered[:rows_chunk]
        if h == 0:
            info_all = gathered[rows_chunk:].reshape(info_rows, n_tp, cols)
            info_all = jnp.transpose(info_all, (1, 0, 2)).reshape(n_tp, tok_blk, info_cols)
            info_all = info_all.astype(jnp.float32)
            expert_all = info_all[:, :, 0:top].astype(jnp.int32)
            slot_all = info_all[:, :, top:2 * top].astype(jnp.int32)
            gates_all = (
                info_all[:, :, 2 * top:3 * top] + info_all[:, :, 3 * top:4 * top]
            ) + info_all[:, :, 4 * top:5 * top]
            dest_ctx = expert_all // (n_tp * exp_dev)
            dest_tp = (expert_all // exp_dev) % n_tp
            dest_loc = expert_all % exp_dev
            mine = dest_tp == me_tp

        blocks = slice(h * blk_chunk, (h + 1) * blk_chunk)
        b_loc = jnp.arange(blk_chunk, dtype=jnp.int32)[:, None, None]
        position = ((dest_ctx[blocks] * blk_chunk + b_loc) * exp_dev + dest_loc[blocks]) * capacity
        position = jnp.where(mine[blocks], position + slot_all[blocks], -1)
        n_rows = n_ctx * blk_chunk * per_dest
        hits = position[..., None] == jnp.arange(n_rows, dtype=jnp.int32)
        select = jnp.sum(hits.astype(jnp.int32), axis=2).astype(jnp.bfloat16)
        weight = jnp.sum(jnp.where(hits, gates_all[blocks][..., None], 0.0), axis=2)
        select = select.reshape(rows_chunk, n_rows)
        weight = weight.reshape(rows_chunk, n_rows)

        outgoing = jnp.einsum(
            "tr,td->rd", select, feats, preferred_element_type=jnp.bfloat16
        ).reshape(n_ctx, blk_chunk * per_dest, width)
        received = lax.all_to_all(outgoing, "ctx", split_axis=0, concat_axis=0, tiled=True)
        rows = received.reshape(n_ctx * blk_chunk, exp_dev, capacity, width)
        rows = jnp.transpose(rows, (1, 0, 2, 3)).reshape(exp_dev, n_ctx * blk_chunk * capacity, width)
        result = expert_rows(rows, w_gate, w_up, w_down, "lsd")
        result = jnp.transpose(
            result.reshape(exp_dev, n_ctx * blk_chunk, capacity, width), (1, 0, 2, 3)
        ).reshape(n_ctx, blk_chunk * per_dest, width)
        returned = lax.all_to_all(result, "ctx", split_axis=0, concat_axis=0, tiled=True)
        returned = returned.reshape(n_rows, width)

        w_hi_f = bf16_part(weight)
        w_hi = w_hi_f.astype(jnp.bfloat16)
        w_lo = (weight - w_hi_f).astype(jnp.bfloat16)
        partial = jnp.dot(w_hi, returned, preferred_element_type=jnp.float32) + jnp.dot(
            w_lo, returned, preferred_element_type=jnp.float32
        )
        outs.append(lax.psum_scatter(partial, "tp", scatter_dimension=1, tiled=True))
    total = jnp.concatenate(outs, axis=0)
    return total.astype(jnp.bfloat16)


def solution(mesh):
    in_specs = (
        P(("dp", "ctx"), "tp"),
        P(("dp", "ctx", "tp"), None),
        P(("dp", "ctx", "tp"), None),
        P(("dp", "ctx", "tp"), None, None),
        P(("dp", "ctx", "tp"), None, None),
        P(("dp", "ctx", "tp"), None, None),
    )
    out_specs = P(("dp", "ctx"), "tp")
    return jax.shard_map(
        on_device, mesh=mesh, in_specs=in_specs, out_specs=out_specs, check_vma=False
    )
```

```python
import jax
import jax.numpy as jnp
from jax import lax
from jax.sharding import PartitionSpec as P

CHUNKS = 2


def slot_numbers(expert_ids, experts):
    one_hot = (
        expert_ids[:, :, None] == jnp.arange(experts, dtype=jnp.int32)[None, None, :]
    ).astype(jnp.int32)
    return jnp.sum(jnp.cumsum(one_hot, axis=1) * one_hot, axis=2) - 1


def expert_rows(features, w_gate, w_up, w_down, form):
    hidden_form = form[:-1] + "f"
    gate_proj = jnp.einsum(
        form + ",ldf->" + hidden_form, features, w_gate, preferred_element_type=jnp.float32
    )
    up_proj = jnp.einsum(
        form + ",ldf->" + hidden_form, features, w_up, preferred_element_type=jnp.float32
    )
    hidden = (jax.nn.silu(gate_proj) * up_proj).astype(jnp.bfloat16)
    result = jnp.einsum(
        hidden_form + ",lfd->" + form, hidden, w_down, preferred_element_type=jnp.float32
    )
    return result.astype(jnp.bfloat16)


def bf16_part(x):
    return lax.reduce_precision(x, exponent_bits=8, mantissa_bits=7)


def on_device(attn_out, routing, gates, w_gate, w_up, w_down):
    n_ctx = lax.axis_size("ctx")
    n_tp = lax.axis_size("tp")
    me_tp = lax.axis_index("tp")
    exp_dev = w_gate.shape[0]
    experts = exp_dev * n_ctx * n_tp
    tok_blk, top = routing.shape
    cols = attn_out.shape[1]
    width = cols * n_tp
    capacity = 3 * tok_blk * top // (2 * experts)
    per_dest = exp_dev * capacity

    slot_of = slot_numbers(routing.reshape(1, tok_blk * top), experts).reshape(tok_blk, top)
    g1 = bf16_part(gates)
    rest = gates - g1
    g2 = bf16_part(rest)
    g3 = rest - g2
    info = jnp.concatenate(
        [routing.astype(jnp.float32), slot_of.astype(jnp.float32), g1, g2, g3], axis=1
    ).astype(jnp.bfloat16)
    info_cols = 64
    info = jnp.pad(info, ((0, 0), (0, info_cols - info.shape[1])))
    info_rows = tok_blk * info_cols // cols
    info = info.reshape(info_rows, cols)

    blk_chunk = n_tp // CHUNKS
    rows_chunk = blk_chunk * tok_blk
    outs = []
    for h in range(CHUNKS):
        piece = attn_out[h * rows_chunk:(h + 1) * rows_chunk]
        if h == 0:
            piece = jnp.concatenate([piece, info], axis=0)
        gathered = lax.all_gather(piece, "tp", axis=1, tiled=True)
        feats = gathered[:rows_chunk]
        if h == 0:
            info_all = gathered[rows_chunk:].reshape(info_rows, n_tp, cols)
            info_all = jnp.transpose(info_all, (1, 0, 2)).reshape(n_tp, tok_blk, info_cols)
            info_all = info_all.astype(jnp.float32)
            expert_all = info_all[:, :, 0:top].astype(jnp.int32)
            slot_all = info_all[:, :, top:2 * top].astype(jnp.int32)
            gates_all = (
                info_all[:, :, 2 * top:3 * top] + info_all[:, :, 3 * top:4 * top]
            ) + info_all[:, :, 4 * top:5 * top]
            dest_ctx = expert_all // (n_tp * exp_dev)
            dest_tp = (expert_all // exp_dev) % n_tp
            dest_loc = expert_all % exp_dev
            mine = dest_tp == me_tp

        blocks = slice(h * blk_chunk, (h + 1) * blk_chunk)
        b_loc = jnp.arange(blk_chunk, dtype=jnp.int32)[:, None, None]
        position = ((dest_ctx[blocks] * blk_chunk + b_loc) * exp_dev + dest_loc[blocks]) * capacity
        position = jnp.where(mine[blocks], position + slot_all[blocks], -1)
        position = jnp.transpose(position.reshape(rows_chunk, top))
        g_chunk = jnp.transpose(gates_all[blocks].reshape(rows_chunk, top))
        g_hi_f = bf16_part(g_chunk)
        g_hi = g_hi_f.astype(jnp.bfloat16)
        g_lo = (g_chunk - g_hi_f).astype(jnp.bfloat16)
        n_rows = n_ctx * blk_chunk * per_dest
        row_ids = jnp.arange(n_rows, dtype=jnp.int32)
        select = sum(
            (position[k][None, :] == row_ids[:, None]).astype(jnp.bfloat16) for k in range(top)
        )
        zero = jnp.zeros((), jnp.bfloat16)
        w_hi = sum(
            jnp.where(position[k][:, None] == row_ids[None, :], g_hi[k][:, None], zero)
            for k in range(top)
        )
        w_lo = sum(
            jnp.where(position[k][:, None] == row_ids[None, :], g_lo[k][:, None], zero)
            for k in range(top)
        )

        outgoing = jnp.dot(
            select, feats, preferred_element_type=jnp.bfloat16
        ).reshape(n_ctx, blk_chunk * per_dest, width)
        received = lax.all_to_all(outgoing, "ctx", split_axis=0, concat_axis=0, tiled=True)
        rows = received.reshape(n_ctx * blk_chunk, exp_dev, capacity, width)
        rows = jnp.transpose(rows, (1, 0, 2, 3)).reshape(exp_dev, n_ctx * blk_chunk * capacity, width)
        result = expert_rows(rows, w_gate, w_up, w_down, "lsd")
        result = jnp.transpose(
            result.reshape(exp_dev, n_ctx * blk_chunk, capacity, width), (1, 0, 2, 3)
        ).reshape(n_ctx, blk_chunk * per_dest, width)
        returned = lax.all_to_all(result, "ctx", split_axis=0, concat_axis=0, tiled=True)
        returned = returned.reshape(n_rows, width)

        partial = jnp.dot(w_hi, returned, preferred_element_type=jnp.float32) + jnp.dot(
            w_lo, returned, preferred_element_type=jnp.float32
        )
        partial = partial.astype(jnp.bfloat16)
        outs.append(lax.psum_scatter(partial, "tp", scatter_dimension=1, tiled=True))
    return jnp.concatenate(outs, axis=0)


def solution(mesh):
    in_specs = (
        P(("dp", "ctx"), "tp"),
        P(("dp", "ctx", "tp"), None),
        P(("dp", "ctx", "tp"), None),
        P(("dp", "ctx", "tp"), None, None),
        P(("dp", "ctx", "tp"), None, None),
        P(("dp", "ctx", "tp"), None, None),
    )
    out_specs = P(("dp", "ctx"), "tp")
    return jax.shard_map(
        on_device, mesh=mesh, in_specs=in_specs, out_specs=out_specs, check_vma=False
    )
```

```python
import jax
import jax.numpy as jnp
from jax import lax
from jax.sharding import PartitionSpec as P

CHUNKS = 2


def slot_numbers(expert_ids, experts):
    one_hot = (
        expert_ids[:, :, None] == jnp.arange(experts, dtype=jnp.int32)[None, None, :]
    ).astype(jnp.int32)
    return jnp.sum(jnp.cumsum(one_hot, axis=1) * one_hot, axis=2) - 1


def expert_rows(features, w_gate, w_up, w_down, form):
    hidden_form = form[:-1] + "f"
    gate_proj = jnp.einsum(
        form + ",ldf->" + hidden_form, features, w_gate, preferred_element_type=jnp.float32
    )
    up_proj = jnp.einsum(
        form + ",ldf->" + hidden_form, features, w_up, preferred_element_type=jnp.float32
    )
    hidden = (jax.nn.silu(gate_proj) * up_proj).astype(jnp.bfloat16)
    result = jnp.einsum(
        hidden_form + ",lfd->" + form, hidden, w_down, preferred_element_type=jnp.float32
    )
    return result.astype(jnp.bfloat16)


def bf16_part(x):
    return lax.reduce_precision(x, exponent_bits=8, mantissa_bits=7)


def on_device(attn_out, routing, gates, w_gate, w_up, w_down):
    n_ctx = lax.axis_size("ctx")
    n_tp = lax.axis_size("tp")
    me_tp = lax.axis_index("tp")
    exp_dev = w_gate.shape[0]
    experts = exp_dev * n_ctx * n_tp
    tok_blk, top = routing.shape
    cols = attn_out.shape[1]
    width = cols * n_tp
    capacity = 3 * tok_blk * top // (2 * experts)
    per_dest = exp_dev * capacity

    slot_of = slot_numbers(routing.reshape(1, tok_blk * top), experts).reshape(tok_blk, top)
    g1 = bf16_part(gates)
    rest = gates - g1
    g2 = bf16_part(rest)
    g3 = rest - g2
    info = jnp.concatenate(
        [routing.astype(jnp.float32), slot_of.astype(jnp.float32), g1, g2, g3], axis=1
    ).astype(jnp.bfloat16)
    info_cols = 64
    info = jnp.pad(info, ((0, 0), (0, info_cols - info.shape[1])))
    info_rows = tok_blk * info_cols // cols
    info = info.reshape(info_rows, cols)

    blk_chunk = n_tp // CHUNKS
    rows_chunk = blk_chunk * tok_blk
    outs = []
    partials = []
    for h in range(CHUNKS):
        piece = attn_out[h * rows_chunk:(h + 1) * rows_chunk]
        if h == 0:
            piece = jnp.concatenate([piece, info], axis=0)
        gathered = lax.all_gather(piece, "tp", axis=0)
        feats = jnp.transpose(gathered[:, :rows_chunk], (1, 0, 2)).reshape(rows_chunk, width)
        if h == 0:
            info_all = gathered[:, rows_chunk:].reshape(n_tp, tok_blk, info_cols)
            info_all = info_all.astype(jnp.float32)
            expert_all = info_all[:, :, 0:top].astype(jnp.int32)
            slot_all = info_all[:, :, top:2 * top].astype(jnp.int32)
            gates_all = (
                info_all[:, :, 2 * top:3 * top] + info_all[:, :, 3 * top:4 * top]
            ) + info_all[:, :, 4 * top:5 * top]
            dest_ctx = expert_all // (n_tp * exp_dev)
            dest_tp = (expert_all // exp_dev) % n_tp
            dest_loc = expert_all % exp_dev
            mine = dest_tp == me_tp

        blocks = slice(h * blk_chunk, (h + 1) * blk_chunk)
        b_loc = jnp.arange(blk_chunk, dtype=jnp.int32)[:, None, None]
        position = ((dest_ctx[blocks] * blk_chunk + b_loc) * exp_dev + dest_loc[blocks]) * capacity
        position = jnp.where(mine[blocks], position + slot_all[blocks], -1)
        position = jnp.transpose(position.reshape(rows_chunk, top))
        g_chunk = jnp.transpose(gates_all[blocks].reshape(rows_chunk, top))
        g_hi_f = bf16_part(g_chunk)
        g_hi = g_hi_f.astype(jnp.bfloat16)
        g_lo = (g_chunk - g_hi_f).astype(jnp.bfloat16)
        n_rows = n_ctx * blk_chunk * per_dest
        row_ids = jnp.arange(n_rows, dtype=jnp.int32)
        select = sum(
            (position[k][None, :] == row_ids[:, None]).astype(jnp.bfloat16) for k in range(top)
        )
        zero = jnp.zeros((), jnp.bfloat16)
        w_both = jnp.concatenate([
            sum(
                jnp.where(position[k][:, None] == row_ids[None, :], g_part[k][:, None], zero)
                for k in range(top)
            )
            for g_part in (g_hi, g_lo)
        ], axis=1)

        outgoing = jnp.dot(
            select, feats, preferred_element_type=jnp.bfloat16
        ).reshape(n_ctx, blk_chunk * per_dest, width)
        received = lax.all_to_all(outgoing, "ctx", split_axis=0, concat_axis=0, tiled=True)
        rows = received.reshape(n_ctx * blk_chunk, exp_dev, capacity, width)
        rows = jnp.transpose(rows, (1, 0, 2, 3)).reshape(exp_dev, n_ctx * blk_chunk * capacity, width)
        result = expert_rows(rows, w_gate, w_up, w_down, "lsd")
        if h > 0:
            result, earlier = lax.optimization_barrier((result, partials[-1]))
            outs.append(lax.psum_scatter(earlier, "tp", scatter_dimension=1, tiled=True))
        result = jnp.transpose(
            result.reshape(exp_dev, n_ctx * blk_chunk, capacity, width), (1, 0, 2, 3)
        ).reshape(n_ctx, blk_chunk * per_dest, width)
        returned = lax.all_to_all(result, "ctx", split_axis=0, concat_axis=0, tiled=True)
        returned = returned.reshape(n_rows, width)

        partial = jnp.dot(
            w_both, jnp.concatenate([returned, returned], axis=0), preferred_element_type=jnp.float32
        ).astype(jnp.bfloat16)
        partials.append(partial)
    outs.append(lax.psum_scatter(partials[-1], "tp", scatter_dimension=1, tiled=True))
    return jnp.concatenate(outs, axis=0)


def solution(mesh):
    in_specs = (
        P(("dp", "ctx"), "tp"),
        P(("dp", "ctx", "tp"), None),
        P(("dp", "ctx", "tp"), None),
        P(("dp", "ctx", "tp"), None, None),
        P(("dp", "ctx", "tp"), None, None),
        P(("dp", "ctx", "tp"), None, None),
    )
    out_specs = P(("dp", "ctx"), "tp")
    return jax.shard_map(
        on_device, mesh=mesh, in_specs=in_specs, out_specs=out_specs, check_vma=False
    )
```

```python
import jax
import jax.numpy as jnp
from jax import lax
from jax.sharding import PartitionSpec as P

CHUNKS = 2


def slot_numbers(expert_ids, experts):
    one_hot = (
        expert_ids[:, :, None] == jnp.arange(experts, dtype=jnp.int32)[None, None, :]
    ).astype(jnp.int32)
    return jnp.sum(jnp.cumsum(one_hot, axis=1) * one_hot, axis=2) - 1


def expert_rows(features, w_gate, w_up, w_down, form):
    hidden_form = form[:-1] + "f"
    gate_proj = jnp.einsum(
        form + ",ldf->" + hidden_form, features, w_gate, preferred_element_type=jnp.float32
    )
    up_proj = jnp.einsum(
        form + ",ldf->" + hidden_form, features, w_up, preferred_element_type=jnp.float32
    )
    hidden = (jax.nn.silu(gate_proj) * up_proj).astype(jnp.bfloat16)
    result = jnp.einsum(
        hidden_form + ",lfd->" + form, hidden, w_down, preferred_element_type=jnp.float32
    )
    return result.astype(jnp.bfloat16)


def bf16_part(x):
    return lax.reduce_precision(x, exponent_bits=8, mantissa_bits=7)


def on_device(attn_out, routing, gates, w_gate, w_up, w_down):
    n_ctx = lax.axis_size("ctx")
    n_tp = lax.axis_size("tp")
    me_tp = lax.axis_index("tp")
    exp_dev = w_gate.shape[0]
    experts = exp_dev * n_ctx * n_tp
    tok_blk, top = routing.shape
    cols = attn_out.shape[1]
    width = cols * n_tp
    capacity = 3 * tok_blk * top // (2 * experts)
    per_dest = exp_dev * capacity

    slot_of = slot_numbers(routing.reshape(1, tok_blk * top), experts).reshape(tok_blk, top)
    g1 = bf16_part(gates)
    rest = gates - g1
    g2 = bf16_part(rest)
    g3 = rest - g2
    info = jnp.concatenate(
        [routing.astype(jnp.float32), slot_of.astype(jnp.float32), g1, g2, g3], axis=1
    ).astype(jnp.bfloat16)
    info_cols = 64
    info = jnp.pad(info, ((0, 0), (0, info_cols - info.shape[1])))
    info_rows = tok_blk * info_cols // cols
    info = info.reshape(info_rows, cols)

    blk_chunk = n_tp // CHUNKS
    rows_chunk = blk_chunk * tok_blk
    outs = []
    partials = []
    for h in range(CHUNKS):
        piece = attn_out[h * rows_chunk:(h + 1) * rows_chunk]
        if h == 0:
            piece = jnp.concatenate([piece, info], axis=0)
        gathered = lax.all_gather(piece, "tp", axis=0)
        feats = jnp.transpose(gathered[:, :rows_chunk], (1, 0, 2)).reshape(rows_chunk, width)
        if h == 0:
            info_all = gathered[:, rows_chunk:].reshape(n_tp, tok_blk, info_cols)
            info_all = info_all.astype(jnp.float32)
            expert_all = info_all[:, :, 0:top].astype(jnp.int32)
            slot_all = info_all[:, :, top:2 * top].astype(jnp.int32)
            gates_all = (
                info_all[:, :, 2 * top:3 * top] + info_all[:, :, 3 * top:4 * top]
            ) + info_all[:, :, 4 * top:5 * top]
            dest_ctx = expert_all // (n_tp * exp_dev)
            dest_tp = (expert_all // exp_dev) % n_tp
            dest_loc = expert_all % exp_dev
            mine = dest_tp == me_tp

        blocks = slice(h * blk_chunk, (h + 1) * blk_chunk)
        b_loc = jnp.arange(blk_chunk, dtype=jnp.int32)[:, None, None]
        position = ((dest_ctx[blocks] * blk_chunk + b_loc) * exp_dev + dest_loc[blocks]) * capacity
        position = jnp.where(mine[blocks], position + slot_all[blocks], -1)
        position = jnp.transpose(position.reshape(rows_chunk, top))
        g_chunk = jnp.transpose(gates_all[blocks].reshape(rows_chunk, top))
        g_hi_f = bf16_part(g_chunk)
        g_hi = g_hi_f.astype(jnp.bfloat16)
        g_lo = (g_chunk - g_hi_f).astype(jnp.bfloat16)
        n_rows = n_ctx * blk_chunk * per_dest
        row_ids = jnp.arange(n_rows, dtype=jnp.int32)
        select = sum(
            (position[k][None, :] == row_ids[:, None]).astype(jnp.bfloat16) for k in range(top)
        )
        zero = jnp.zeros((), jnp.bfloat16)
        w_both = jnp.concatenate([
            sum(
                jnp.where(position[k][:, None] == row_ids[None, :], g_part[k][:, None], zero)
                for k in range(top)
            )
            for g_part in (g_hi, g_lo)
        ], axis=0)

        outgoing = jnp.dot(
            select, feats, preferred_element_type=jnp.bfloat16
        ).reshape(n_ctx, blk_chunk * per_dest, width)
        received = lax.all_to_all(outgoing, "ctx", split_axis=0, concat_axis=0, tiled=True)
        rows = received.reshape(n_ctx * blk_chunk, exp_dev, capacity, width)
        rows = jnp.transpose(rows, (1, 0, 2, 3)).reshape(exp_dev, n_ctx * blk_chunk * capacity, width)
        result = expert_rows(rows, w_gate, w_up, w_down, "lsd")
        if h > 0:
            result, earlier = lax.optimization_barrier((result, partials[-1]))
            outs.append(lax.psum_scatter(earlier, "tp", scatter_dimension=1, tiled=True))
        result = jnp.transpose(
            result.reshape(exp_dev, n_ctx * blk_chunk, capacity, width), (1, 0, 2, 3)
        ).reshape(n_ctx, blk_chunk * per_dest, width)
        returned = lax.all_to_all(result, "ctx", split_axis=0, concat_axis=0, tiled=True)
        returned = returned.reshape(n_rows, width)

        both = jnp.dot(w_both, returned, preferred_element_type=jnp.float32)
        partial = (both[:rows_chunk] + both[rows_chunk:]).astype(jnp.bfloat16)
        partials.append(partial)
    outs.append(lax.psum_scatter(partials[-1], "tp", scatter_dimension=1, tiled=True))
    return jnp.concatenate(outs, axis=0)


def solution(mesh):
    in_specs = (
        P(("dp", "ctx"), "tp"),
        P(("dp", "ctx", "tp"), None),
        P(("dp", "ctx", "tp"), None),
        P(("dp", "ctx", "tp"), None, None),
        P(("dp", "ctx", "tp"), None, None),
        P(("dp", "ctx", "tp"), None, None),
    )
    out_specs = P(("dp", "ctx"), "tp")
    return jax.shard_map(
        on_device, mesh=mesh, in_specs=in_specs, out_specs=out_specs, check_vma=False
    )
```

```python
import jax
import jax.numpy as jnp
from jax import lax
from jax.sharding import PartitionSpec as P

CHUNKS = 2


def slot_numbers(expert_ids, experts):
    one_hot = (
        expert_ids[:, :, None] == jnp.arange(experts, dtype=jnp.int32)[None, None, :]
    ).astype(jnp.int32)
    return jnp.sum(jnp.cumsum(one_hot, axis=1) * one_hot, axis=2) - 1


def expert_rows(features, w_gate, w_up, w_down, form):
    hidden_form = form[:-1] + "f"
    gate_proj = jnp.einsum(
        form + ",ldf->" + hidden_form, features, w_gate, preferred_element_type=jnp.float32
    )
    up_proj = jnp.einsum(
        form + ",ldf->" + hidden_form, features, w_up, preferred_element_type=jnp.float32
    )
    hidden = (jax.nn.silu(gate_proj) * up_proj).astype(jnp.bfloat16)
    result = jnp.einsum(
        hidden_form + ",lfd->" + form, hidden, w_down, preferred_element_type=jnp.float32
    )
    return result.astype(jnp.bfloat16)


def bf16_part(x):
    return lax.reduce_precision(x, exponent_bits=8, mantissa_bits=7)


def on_device(attn_out, routing, gates, w_gate, w_up, w_down):
    n_ctx = lax.axis_size("ctx")
    n_tp = lax.axis_size("tp")
    me_tp = lax.axis_index("tp")
    exp_dev = w_gate.shape[0]
    experts = exp_dev * n_ctx * n_tp
    tok_blk, top = routing.shape
    cols = attn_out.shape[1]
    width = cols * n_tp
    capacity = 3 * tok_blk * top // (2 * experts)
    per_dest = exp_dev * capacity

    slot_of = slot_numbers(routing.reshape(1, tok_blk * top), experts).reshape(tok_blk, top)
    info = jnp.concatenate([routing.astype(jnp.float32), slot_of.astype(jnp.float32), gates], axis=1)
    info_all = lax.all_gather(info, "tp", axis=0)
    expert_all = info_all[:, :, 0:top].astype(jnp.int32)
    slot_all = info_all[:, :, top:2 * top].astype(jnp.int32)
    gates_all = info_all[:, :, 2 * top:3 * top]
    dest_ctx = expert_all // (n_tp * exp_dev)
    dest_tp = (expert_all // exp_dev) % n_tp
    dest_loc = expert_all % exp_dev
    mine = dest_tp == me_tp

    blk_chunk = n_tp // CHUNKS
    rows_chunk = blk_chunk * tok_blk
    outs = []
    partials = []
    for h in range(CHUNKS):
        piece = attn_out[h * rows_chunk:(h + 1) * rows_chunk]
        gathered = lax.all_gather(piece, "tp", axis=0)
        feats = jnp.transpose(gathered, (1, 0, 2)).reshape(rows_chunk, width)

        blocks = slice(h * blk_chunk, (h + 1) * blk_chunk)
        b_loc = jnp.arange(blk_chunk, dtype=jnp.int32)[:, None, None]
        position = ((dest_ctx[blocks] * blk_chunk + b_loc) * exp_dev + dest_loc[blocks]) * capacity
        position = jnp.where(mine[blocks], position + slot_all[blocks], -1)
        position = jnp.transpose(position.reshape(rows_chunk, top))
        g_chunk = jnp.transpose(gates_all[blocks].reshape(rows_chunk, top))
        g_hi_f = bf16_part(g_chunk)
        g_hi = g_hi_f.astype(jnp.bfloat16)
        g_lo = (g_chunk - g_hi_f).astype(jnp.bfloat16)
        n_rows = n_ctx * blk_chunk * per_dest
        row_ids = jnp.arange(n_rows, dtype=jnp.int32)
        select = sum(
            (position[k][None, :] == row_ids[:, None]).astype(jnp.bfloat16) for k in range(top)
        )
        zero = jnp.zeros((), jnp.bfloat16)
        w_both = jnp.concatenate([
            sum(
                jnp.where(position[k][:, None] == row_ids[None, :], g_part[k][:, None], zero)
                for k in range(top)
            )
            for g_part in (g_hi, g_lo)
        ], axis=0)

        outgoing = jnp.dot(
            select, feats, preferred_element_type=jnp.bfloat16
        ).reshape(n_ctx, blk_chunk * per_dest, width)
        received = lax.all_to_all(outgoing, "ctx", split_axis=0, concat_axis=0, tiled=True)
        rows = received.reshape(n_ctx * blk_chunk, exp_dev, capacity, width)
        rows = jnp.transpose(rows, (1, 0, 2, 3)).reshape(exp_dev, n_ctx * blk_chunk * capacity, width)
        result = expert_rows(rows, w_gate, w_up, w_down, "lsd")
        if h > 0:
            result, earlier = lax.optimization_barrier((result, partials[-1]))
            outs.append(lax.psum_scatter(earlier, "tp", scatter_dimension=1, tiled=True))
        result = jnp.transpose(
            result.reshape(exp_dev, n_ctx * blk_chunk, capacity, width), (1, 0, 2, 3)
        ).reshape(n_ctx, blk_chunk * per_dest, width)
        returned = lax.all_to_all(result, "ctx", split_axis=0, concat_axis=0, tiled=True)
        returned = returned.reshape(n_rows, width)

        both = jnp.dot(w_both, returned, preferred_element_type=jnp.float32)
        partial = (both[:rows_chunk] + both[rows_chunk:]).astype(jnp.bfloat16)
        partials.append(partial)
    outs.append(lax.psum_scatter(partials[-1], "tp", scatter_dimension=1, tiled=True))
    return jnp.concatenate(outs, axis=0)


def solution(mesh):
    in_specs = (
        P(("dp", "ctx"), "tp"),
        P(("dp", "ctx", "tp"), None),
        P(("dp", "ctx", "tp"), None),
        P(("dp", "ctx", "tp"), None, None),
        P(("dp", "ctx", "tp"), None, None),
        P(("dp", "ctx", "tp"), None, None),
    )
    out_specs = P(("dp", "ctx"), "tp")
    return jax.shard_map(
        on_device, mesh=mesh, in_specs=in_specs, out_specs=out_specs, check_vma=False
    )
```

```python
import jax
import jax.numpy as jnp
from jax import lax
from jax.sharding import PartitionSpec as P

CHUNKS = 2


def slot_numbers(expert_ids, experts):
    one_hot = (
        expert_ids[:, :, None] == jnp.arange(experts, dtype=jnp.int32)[None, None, :]
    ).astype(jnp.int32)
    return jnp.sum(jnp.cumsum(one_hot, axis=1) * one_hot, axis=2) - 1


def expert_rows(features, w_gate, w_up, w_down, form):
    hidden_form = form[:-1] + "f"
    gate_proj = jnp.einsum(
        form + ",ldf->" + hidden_form, features, w_gate, preferred_element_type=jnp.float32
    )
    up_proj = jnp.einsum(
        form + ",ldf->" + hidden_form, features, w_up, preferred_element_type=jnp.float32
    )
    hidden = (jax.nn.silu(gate_proj) * up_proj).astype(jnp.bfloat16)
    result = jnp.einsum(
        hidden_form + ",lfd->" + form, hidden, w_down, preferred_element_type=jnp.float32
    )
    return result.astype(jnp.bfloat16)


def bf16_part(x):
    return lax.reduce_precision(x, exponent_bits=8, mantissa_bits=7)


def on_device(attn_out, routing, gates, w_gate, w_up, w_down):
    n_ctx = lax.axis_size("ctx")
    n_tp = lax.axis_size("tp")
    me_tp = lax.axis_index("tp")
    exp_dev = w_gate.shape[0]
    experts = exp_dev * n_ctx * n_tp
    tok_blk, top = routing.shape
    cols = attn_out.shape[1]
    width = cols * n_tp
    capacity = 3 * tok_blk * top // (2 * experts)
    per_dest = exp_dev * capacity

    slot_of = slot_numbers(routing.reshape(1, tok_blk * top), experts).reshape(tok_blk, top)
    info = jnp.concatenate([routing.astype(jnp.float32), slot_of.astype(jnp.float32), gates], axis=1)
    info_all = lax.all_gather(info, "tp", axis=0)
    expert_all = info_all[:, :, 0:top].astype(jnp.int32)
    slot_all = info_all[:, :, top:2 * top].astype(jnp.int32)
    gates_all = info_all[:, :, 2 * top:3 * top]
    dest_ctx = expert_all // (n_tp * exp_dev)
    dest_tp = (expert_all // exp_dev) % n_tp
    dest_loc = expert_all % exp_dev
    mine = dest_tp == me_tp

    blk_chunk = n_tp // CHUNKS
    rows_chunk = blk_chunk * tok_blk
    outs = []
    partials = []
    for h in range(CHUNKS):
        piece = attn_out[h * rows_chunk:(h + 1) * rows_chunk]
        gathered = lax.all_gather(piece, "tp", axis=0)
        feats = gathered.reshape(n_tp, rows_chunk, cols)

        blocks = slice(h * blk_chunk, (h + 1) * blk_chunk)
        b_loc = jnp.arange(blk_chunk, dtype=jnp.int32)[:, None, None]
        position = ((dest_ctx[blocks] * blk_chunk + b_loc) * exp_dev + dest_loc[blocks]) * capacity
        position = jnp.where(mine[blocks], position + slot_all[blocks], -1)
        position = jnp.transpose(position.reshape(rows_chunk, top))
        g_chunk = jnp.transpose(gates_all[blocks].reshape(rows_chunk, top))
        g_hi_f = bf16_part(g_chunk)
        g_hi = g_hi_f.astype(jnp.bfloat16)
        g_lo = (g_chunk - g_hi_f).astype(jnp.bfloat16)
        n_rows = n_ctx * blk_chunk * per_dest
        row_ids = jnp.arange(n_rows, dtype=jnp.int32)
        select = sum(
            (position[k][None, :] == row_ids[:, None]).astype(jnp.bfloat16) for k in range(top)
        )
        zero = jnp.zeros((), jnp.bfloat16)
        w_both = jnp.concatenate([
            sum(
                jnp.where(position[k][:, None] == row_ids[None, :], g_part[k][:, None], zero)
                for k in range(top)
            )
            for g_part in (g_hi, g_lo)
        ], axis=0)

        outgoing = jnp.einsum(
            "rt,stf->rsf", select, feats, preferred_element_type=jnp.bfloat16
        ).reshape(n_ctx, blk_chunk * per_dest, n_tp, cols)
        received = lax.all_to_all(outgoing, "ctx", split_axis=0, concat_axis=0, tiled=True)
        rows = received.reshape(n_ctx * blk_chunk, exp_dev, capacity, width)
        rows = jnp.transpose(rows, (1, 0, 2, 3)).reshape(exp_dev, n_ctx * blk_chunk * capacity, width)
        result = expert_rows(rows, w_gate, w_up, w_down, "lsd")
        if h > 0:
            result, earlier = lax.optimization_barrier((result, partials[-1]))
            outs.append(lax.psum_scatter(earlier, "tp", scatter_dimension=1, tiled=True))
        result = jnp.transpose(
            result.reshape(exp_dev, n_ctx * blk_chunk, capacity, width), (1, 0, 2, 3)
        ).reshape(n_ctx, blk_chunk * per_dest, width)
        returned = lax.all_to_all(result, "ctx", split_axis=0, concat_axis=0, tiled=True)
        returned = returned.reshape(n_rows, width)

        both = jnp.dot(w_both, returned, preferred_element_type=jnp.float32)
        partial = (both[:rows_chunk] + both[rows_chunk:]).astype(jnp.bfloat16)
        partials.append(partial)
    outs.append(lax.psum_scatter(partials[-1], "tp", scatter_dimension=1, tiled=True))
    return jnp.concatenate(outs, axis=0)


def solution(mesh):
    in_specs = (
        P(("dp", "ctx"), "tp"),
        P(("dp", "ctx", "tp"), None),
        P(("dp", "ctx", "tp"), None),
        P(("dp", "ctx", "tp"), None, None),
        P(("dp", "ctx", "tp"), None, None),
        P(("dp", "ctx", "tp"), None, None),
    )
    out_specs = P(("dp", "ctx"), "tp")
    return jax.shard_map(
        on_device, mesh=mesh, in_specs=in_specs, out_specs=out_specs, check_vma=False
    )
```

```python
import jax
import jax.numpy as jnp
from jax import lax
from jax.sharding import PartitionSpec as P

CHUNKS = 2


def slot_numbers(expert_ids, experts):
    one_hot = (
        expert_ids[:, :, None] == jnp.arange(experts, dtype=jnp.int32)[None, None, :]
    ).astype(jnp.int32)
    return jnp.sum(jnp.cumsum(one_hot, axis=1) * one_hot, axis=2) - 1


def expert_rows(features, w_gate, w_up, w_down, form):
    hidden_form = form[:-1] + "f"
    gate_proj = jnp.einsum(
        form + ",ldf->" + hidden_form, features, w_gate, preferred_element_type=jnp.float32
    )
    up_proj = jnp.einsum(
        form + ",ldf->" + hidden_form, features, w_up, preferred_element_type=jnp.float32
    )
    hidden = (jax.nn.silu(gate_proj) * up_proj).astype(jnp.bfloat16)
    result = jnp.einsum(
        hidden_form + ",lfd->" + form, hidden, w_down, preferred_element_type=jnp.float32
    )
    return result.astype(jnp.bfloat16)


def bf16_part(x):
    return lax.reduce_precision(x, exponent_bits=8, mantissa_bits=7)


def on_device(attn_out, routing, gates, w_gate, w_up, w_down):
    n_ctx = lax.axis_size("ctx")
    n_tp = lax.axis_size("tp")
    me_tp = lax.axis_index("tp")
    exp_dev = w_gate.shape[0]
    experts = exp_dev * n_ctx * n_tp
    tok_blk, top = routing.shape
    cols = attn_out.shape[1]
    width = cols * n_tp
    capacity = 3 * tok_blk * top // (2 * experts)
    per_dest = exp_dev * capacity

    slot_of = slot_numbers(routing.reshape(1, tok_blk * top), experts).reshape(tok_blk, top)
    info = jnp.concatenate([routing.astype(jnp.float32), slot_of.astype(jnp.float32), gates], axis=1)
    info_all = lax.all_gather(info, "tp", axis=0)
    expert_all = info_all[:, :, 0:top].astype(jnp.int32)
    slot_all = info_all[:, :, top:2 * top].astype(jnp.int32)
    gates_all = info_all[:, :, 2 * top:3 * top]
    dest_ctx = expert_all // (n_tp * exp_dev)
    dest_tp = (expert_all // exp_dev) % n_tp
    dest_loc = expert_all % exp_dev
    mine = dest_tp == me_tp

    blk_chunk = n_tp // CHUNKS
    rows_chunk = blk_chunk * tok_blk
    outs = []
    for h in range(CHUNKS):
        piece = attn_out[h * rows_chunk:(h + 1) * rows_chunk]
        gathered = lax.all_gather(piece, "tp", axis=0)
        feats = gathered.reshape(n_tp, rows_chunk, cols)

        blocks = slice(h * blk_chunk, (h + 1) * blk_chunk)
        b_loc = jnp.arange(blk_chunk, dtype=jnp.int32)[:, None, None]
        position = ((dest_ctx[blocks] * blk_chunk + b_loc) * exp_dev + dest_loc[blocks]) * capacity
        position = jnp.where(mine[blocks], position + slot_all[blocks], -1)
        position = jnp.transpose(position.reshape(rows_chunk, top))
        g_chunk = jnp.transpose(gates_all[blocks].reshape(rows_chunk, top))
        g_hi_f = bf16_part(g_chunk)
        g_hi = g_hi_f.astype(jnp.bfloat16)
        g_lo = (g_chunk - g_hi_f).astype(jnp.bfloat16)
        n_rows = n_ctx * blk_chunk * per_dest
        row_ids = jnp.arange(n_rows, dtype=jnp.int32)
        select = sum(
            (position[k][None, :] == row_ids[:, None]).astype(jnp.bfloat16) for k in range(top)
        )
        zero = jnp.zeros((), jnp.bfloat16)
        w_both = jnp.concatenate([
            sum(
                jnp.where(position[k][:, None] == row_ids[None, :], g_part[k][:, None], zero)
                for k in range(top)
            )
            for g_part in (g_hi, g_lo)
        ], axis=0)

        outgoing = jnp.einsum(
            "rt,stf->rsf", select, feats, preferred_element_type=jnp.bfloat16
        ).reshape(n_ctx, blk_chunk * per_dest, n_tp, cols)
        received = lax.all_to_all(outgoing, "ctx", split_axis=0, concat_axis=0, tiled=True)
        rows = received.reshape(n_ctx * blk_chunk, exp_dev, capacity, width)
        rows = jnp.transpose(rows, (1, 0, 2, 3)).reshape(exp_dev, n_ctx * blk_chunk * capacity, width)
        result = expert_rows(rows, w_gate, w_up, w_down, "lsd")
        result = jnp.transpose(
            result.reshape(exp_dev, n_ctx * blk_chunk, capacity, width), (1, 0, 2, 3)
        ).reshape(n_ctx, blk_chunk * per_dest, width)
        returned = lax.all_to_all(result, "ctx", split_axis=0, concat_axis=0, tiled=True)
        returned = returned.reshape(n_rows, width)

        both = jnp.dot(w_both, returned, preferred_element_type=jnp.float32)
        partial = (both[:rows_chunk] + both[rows_chunk:]).astype(jnp.bfloat16)
        outs.append(lax.psum_scatter(partial, "tp", scatter_dimension=1, tiled=True))
    return jnp.concatenate(outs, axis=0)


def solution(mesh):
    in_specs = (
        P(("dp", "ctx"), "tp"),
        P(("dp", "ctx", "tp"), None),
        P(("dp", "ctx", "tp"), None),
        P(("dp", "ctx", "tp"), None, None),
        P(("dp", "ctx", "tp"), None, None),
        P(("dp", "ctx", "tp"), None, None),
    )
    out_specs = P(("dp", "ctx"), "tp")
    return jax.shard_map(
        on_device, mesh=mesh, in_specs=in_specs, out_specs=out_specs, check_vma=False
    )
```

```python
import jax
import jax.numpy as jnp
from jax import lax
from jax.sharding import PartitionSpec as P

CHUNKS = 2


def slot_numbers(expert_ids, experts):
    one_hot = (
        expert_ids[:, :, None] == jnp.arange(experts, dtype=jnp.int32)[None, None, :]
    ).astype(jnp.int32)
    return jnp.sum(jnp.cumsum(one_hot, axis=1) * one_hot, axis=2) - 1


def expert_rows(features, w_gate, w_up, w_down, form):
    hidden_form = form[:-1] + "f"
    gate_proj = jnp.einsum(
        form + ",ldf->" + hidden_form, features, w_gate, preferred_element_type=jnp.float32
    )
    up_proj = jnp.einsum(
        form + ",ldf->" + hidden_form, features, w_up, preferred_element_type=jnp.float32
    )
    hidden = (jax.nn.silu(gate_proj) * up_proj).astype(jnp.bfloat16)
    result = jnp.einsum(
        hidden_form + ",lfd->" + form, hidden, w_down, preferred_element_type=jnp.float32
    )
    return result.astype(jnp.bfloat16)


def bf16_part(x):
    return lax.reduce_precision(x, exponent_bits=8, mantissa_bits=7)


def on_device(attn_out, routing, gates, w_gate, w_up, w_down):
    n_ctx = lax.axis_size("ctx")
    n_tp = lax.axis_size("tp")
    me_tp = lax.axis_index("tp")
    exp_dev = w_gate.shape[0]
    experts = exp_dev * n_ctx * n_tp
    tok_blk, top = routing.shape
    cols = attn_out.shape[1]
    width = cols * n_tp
    capacity = 3 * tok_blk * top // (2 * experts)
    per_dest = exp_dev * capacity

    slot_of = slot_numbers(routing.reshape(1, tok_blk * top), experts).reshape(tok_blk, top)
    info = jnp.concatenate([routing.astype(jnp.float32), slot_of.astype(jnp.float32), gates], axis=1)
    info_all = lax.all_gather(info, "tp", axis=0)
    expert_all = info_all[:, :, 0:top].astype(jnp.int32)
    slot_all = info_all[:, :, top:2 * top].astype(jnp.int32)
    gates_all = info_all[:, :, 2 * top:3 * top]
    dest_ctx = expert_all // (n_tp * exp_dev)
    dest_tp = (expert_all // exp_dev) % n_tp
    dest_loc = expert_all % exp_dev
    mine = dest_tp == me_tp

    blk_chunk = n_tp // CHUNKS
    rows_chunk = blk_chunk * tok_blk
    outs = []
    for h in range(CHUNKS):
        piece = attn_out[h * rows_chunk:(h + 1) * rows_chunk]
        gathered = lax.all_gather(piece, "tp", axis=0)
        feats = gathered.reshape(n_tp, rows_chunk, cols)

        blocks = slice(h * blk_chunk, (h + 1) * blk_chunk)
        b_loc = jnp.arange(blk_chunk, dtype=jnp.int32)[:, None, None]
        position = ((dest_ctx[blocks] * blk_chunk + b_loc) * exp_dev + dest_loc[blocks]) * capacity
        position = jnp.where(mine[blocks], position + slot_all[blocks], -1)
        position = jnp.transpose(position.reshape(rows_chunk, top))
        g_chunk = jnp.transpose(gates_all[blocks].reshape(rows_chunk, top))
        g_hi_f = bf16_part(g_chunk)
        g_hi = g_hi_f.astype(jnp.bfloat16)
        g_lo = (g_chunk - g_hi_f).astype(jnp.bfloat16)
        n_rows = n_ctx * blk_chunk * per_dest
        row_ids = jnp.arange(n_rows, dtype=jnp.int32)
        select = sum(
            (position[k][None, :] == row_ids[:, None]).astype(jnp.bfloat16) for k in range(top)
        )
        zero = jnp.zeros((), jnp.bfloat16)
        w_both = jnp.concatenate([
            sum(
                jnp.where(position[k][:, None] == row_ids[None, :], g_part[k][:, None], zero)
                for k in range(top)
            )
            for g_part in (g_hi, g_lo)
        ], axis=0)

        select = lax.optimization_barrier(select)
        outgoing = jnp.einsum(
            "rt,stf->rsf", select, feats, preferred_element_type=jnp.bfloat16
        ).reshape(n_ctx, blk_chunk * per_dest, n_tp, cols)
        received = lax.all_to_all(outgoing, "ctx", split_axis=0, concat_axis=0, tiled=True)
        rows = received.reshape(n_ctx * blk_chunk, exp_dev, capacity, width)
        rows = jnp.transpose(rows, (1, 0, 2, 3)).reshape(exp_dev, n_ctx * blk_chunk * capacity, width)
        result = expert_rows(rows, w_gate, w_up, w_down, "lsd")
        result = jnp.transpose(
            result.reshape(exp_dev, n_ctx * blk_chunk, capacity, width), (1, 0, 2, 3)
        ).reshape(n_ctx, blk_chunk * per_dest, width)
        returned = lax.all_to_all(result, "ctx", split_axis=0, concat_axis=0, tiled=True)
        returned = returned.reshape(n_rows, width)

        both = jnp.dot(w_both, returned, preferred_element_type=jnp.float32)
        partial = (both[:rows_chunk] + both[rows_chunk:]).astype(jnp.bfloat16)
        outs.append(lax.psum_scatter(partial, "tp", scatter_dimension=1, tiled=True))
    return jnp.concatenate(outs, axis=0)


def solution(mesh):
    in_specs = (
        P(("dp", "ctx"), "tp"),
        P(("dp", "ctx", "tp"), None),
        P(("dp", "ctx", "tp"), None),
        P(("dp", "ctx", "tp"), None, None),
        P(("dp", "ctx", "tp"), None, None),
        P(("dp", "ctx", "tp"), None, None),
    )
    out_specs = P(("dp", "ctx"), "tp")
    return jax.shard_map(
        on_device, mesh=mesh, in_specs=in_specs, out_specs=out_specs, check_vma=False
    )
```
